128 devices in a mesh: row: 8 (over y, core), col: 16 (over x, z).
Axes of the slice: x: 4, y: 4, z: 4, core: 2. Of those that a mesh axis runs over, the one named last changes fastest.
Arguments:
- tokens: bfloat16 [10240, 3200], P('col', 'row'), may hold values from -24 to 24
- w_qkv: bfloat16 [3200, 9600], P('row', 'col'), may hold values from -4 to 4
- q_gain: float32 [3200], replicated, may hold values from 0.5 to 1.5
- k_gain: float32 [3200], replicated, may hold values from 0.5 to 1.5
- segment_ids: int32 [8, 1280], P('row'), may hold values from 0 to 3, never falling along the last dimension, each value on 1 to 640 neighbouring positions
Outputs:
- attended: bfloat16 [10240, 3200], P(('row', 'col'))
The draws below stay inside these ranges and needn't reach their ends.
Inputs may be any that keep to these rules, and one draw needn't show every extreme that they name: `segment_ids`: in each pack the ids never fall; each of the 4 images holds 1 to 640 tokens, one exactly 640.
All inputs are finite; a program needn't handle non-finite values.
Results may differ from the reference program's by a relative error of at most 0.033.
Values may be sent and summed in bfloat16 or wider, within the bound.
No kernel may reach another device: no remote copies, remote signals or barrier semaphores. Data moves between devices by JAX's collectives and lax.ppermute only.
A program may use at most 192 MiB of HBM per device.

```python
import math
import jax
import jax.numpy as jnp
import numpy as np
from jax import lax

ATTENTION_HEADS = 25
HEAD_WIDTH = 128
D = 3200
SEGS = 4
PACK_TOKENS = 1280
PACKS = 8
TOKENS = 10240
MOST = 640
N_ROW = 8


def draw_tokens(key, part):
    key_base = jax.random.fold_in(key, 0)
    values = jnp.clip(jax.random.normal(key_base, (TOKENS, D), jnp.float32), -6.0, 6.0)
    return values.astype(jnp.bfloat16)


def draw_w_qkv(key, part):
    key_base = jax.random.fold_in(key, 0)
    spread = D ** (-0.5)
    base = jax.random.normal(key_base, (D, 3 * D), jnp.float32) * spread
    return jnp.clip(base, -4.0, 4.0).astype(jnp.bfloat16)


def length_profile(amount, total, most, slope):
    loads = [(1 << 20) // math.isqrt(standing ** slope) + 1 for standing in range(2, amount + 1)]
    rest, holding = total - most - (amount - 1), [1] * (amount - 1)
    while rest > 0:
        movable = [i for i in range(amount - 1) if holding[i] < most]
        pool, left = sum([loads[i] for i in movable]), rest
        for i in movable:
            addition = min(most - holding[i], max(1, left * loads[i] // pool), rest)
            holding[i] = holding[i] + addition
            rest = rest - addition
    return np.array([most] + holding)


def uneven(own_key, amount, total, limit, slope):
    if amount == 2:
        one = jax.random.randint(own_key, (), max(1, total - limit), min(limit, total - 1) + 1)
        return jnp.stack([one, total - one])
    sizes = jnp.asarray(length_profile(amount, total, limit, slope), jnp.int32)
    twos = (amount - 1) // 2
    giver, receiver = sizes[1:1 + 2 * twos:2], sizes[2:2 + 2 * twos:2]
    slack = jnp.minimum(giver - 1, limit - receiver)
    passed = jax.random.randint(jax.random.fold_in(own_key, 1), (twos,), 0, 1 << 20) % (slack + 1)
    sizes = sizes.at[1:1 + 2 * twos:2].set(giver - passed).at[2:2 + 2 * twos:2].set(receiver + passed)
    return sizes[jax.random.permutation(jax.random.fold_in(own_key, 2), amount)]


def setup_inputs(seed: int = 0) -> dict:
    seeds = jax.random.split(jax.random.key(seed), 6)
    tokens = draw_tokens(jax.random.fold_in(seeds[5], 71), 0)
    w_qkv = draw_w_qkv(jax.random.fold_in(seeds[5], 71), 0)
    q_gain = jnp.clip(1.0 + 0.1 * jax.random.normal(seeds[2], (D,), jnp.float32), 0.5, 1.5)
    k_gain = jnp.clip(1.0 + 0.1 * jax.random.normal(seeds[3], (D,), jnp.float32), 0.5, 1.5)
    segment_ids = jax.vmap(lambda own: jnp.searchsorted(jnp.cumsum(uneven(own, SEGS, PACK_TOKENS, MOST, 2)), jnp.arange(PACK_TOKENS), side="right"))(jax.random.split(seeds[4], PACKS)).reshape((PACKS, PACK_TOKENS)).astype(jnp.int32)
    return {"tokens": tokens, "w_qkv": w_qkv, "q_gain": q_gain, "k_gain": k_gain, "segment_ids": segment_ids}


def rms_norm(block, gain):
    values = block.astype(jnp.float32)
    mean_sq = lax.optimization_barrier(jnp.mean(values * values, axis=-1, keepdims=True))
    return (values * lax.rsqrt(mean_sq + 1e-06) * gain.astype(jnp.float32)).astype(jnp.bfloat16)

def reference(tokens, w_qkv, q_gain, k_gain, segment_ids):
    width = tokens.shape[1]
    block_width = width // N_ROW

    def add_block(index, accum):
        cols = lax.dynamic_slice_in_dim(tokens, index * block_width, block_width, 1)
        rows = lax.dynamic_slice_in_dim(w_qkv, index * block_width, block_width, 0)
        part = jnp.dot(cols, rows, preferred_element_type=jnp.float32)
        part = lax.optimization_barrier(part.astype(jnp.bfloat16)).astype(jnp.float32)
        return accum + part
    start_acc = jnp.zeros((tokens.shape[0], w_qkv.shape[1]), jnp.float32)
    qkv = lax.fori_loop(0, N_ROW, add_block, start_acc).astype(jnp.bfloat16)
    normed_q = rms_norm(qkv[:, :width], q_gain)
    normed_k = rms_norm(qkv[:, width:2 * width], k_gain)
    values = qkv[:, 2 * width:]
    scale = HEAD_WIDTH ** (-0.5)

    def one_pack(pack_entry):
        query_packed, key_packed, value_packed, token_labels = pack_entry
        q3 = query_packed.reshape(PACK_TOKENS, ATTENTION_HEADS, HEAD_WIDTH).astype(jnp.float32)
        k3 = key_packed.reshape(PACK_TOKENS, ATTENTION_HEADS, HEAD_WIDTH).astype(jnp.float32)
        value_three = value_packed.reshape(PACK_TOKENS, ATTENTION_HEADS, HEAD_WIDTH).astype(jnp.float32)
        scores = jnp.einsum('qhd,khd->hqk', q3, k3) * scale
        mask = (token_labels[:, None] == token_labels[None, :])[None]
        masked = jnp.where(mask, scores, -1e+30)
        top = lax.optimization_barrier(jnp.max(masked, axis=-1, keepdims=True))
        expo = jnp.where(mask, jnp.exp(masked - top), 0.0)
        total = lax.optimization_barrier(jnp.sum(expo, axis=-1))
        weights = expo.astype(jnp.bfloat16).astype(jnp.float32)
        summed = jnp.einsum('hqk,khd->hqd', weights, value_three)
        result = summed / total[..., None]
        return jnp.transpose(result, (1, 0, 2)).reshape(PACK_TOKENS, ATTENTION_HEADS * HEAD_WIDTH).astype(jnp.bfloat16)
    packed = (normed_q.reshape(PACKS, PACK_TOKENS, width), normed_k.reshape(PACKS, PACK_TOKENS, width), values.reshape(PACKS, PACK_TOKENS, width), segment_ids)
    return lax.map(one_pack, packed).reshape(PACKS * PACK_TOKENS, width)
```

```python
import numpy as np
import jax
import jax.numpy as jnp
from jax import lax
from jax.sharding import Mesh, PartitionSpec as P

ATTENTION_HEADS = 25
HEAD_WIDTH = 128
ROW = ("y", "k")
COL = ("x", "z")


def build_local(nx, nz):
    nc = nx * nz

    def col_of_rho(rho):
        return (rho % nx) * nz + rho // nx

    perms, regions = [], np.zeros((nc, 3), np.int32)
    for j in range(3):
        pairs = []
        for src in range(nc):
            rho = (3 * src + j) % nc
            regions[rho, j] = (3 * src + j) // nc
            pairs.append((src, col_of_rho(rho)))
        perms.append(pairs)
    assert all(sorted(regions[r]) == [0, 1, 2] for r in range(nc))

    def head_table(width):
        piece = width // nc
        h0 = np.zeros(nc, np.int32)
        off = np.zeros((nc, 2), np.int32)
        owner = []
        for rho in range(nc):
            lo, hi = piece * rho, piece * (rho + 1)
            hs = [h for h in range(ATTENTION_HEADS) if lo <= h * HEAD_WIDTH < hi]
            assert 1 <= len(hs) <= 2
            for slot in range(2):
                o = (hs[0] + slot) * HEAD_WIDTH - lo
                off[rho, slot] = min(o, piece)
            for slot, h in enumerate(hs):
                owner.append((h, col_of_rho(rho), slot))
        owner.sort()
        assert [o[0] for o in owner] == list(range(ATTENTION_HEADS))
        gather = np.array([c * 2 + s for _, c, s in owner], np.int32)
        return off, gather

    shift_pairs = [(col_of_rho(r + 1), col_of_rho(r)) for r in range(nc - 1)]

    def local(tokens, w_qkv, q_gain, k_gain, segment_ids):
        tok_blk, feat_blk = tokens.shape
        width = q_gain.shape[0]
        piece = width // nc
        quarter = tok_blk // nx
        pack_tokens = segment_ids.shape[1]
        x = lax.axis_index("x")
        z = lax.axis_index("z")
        rho = z * nx + x
        off_tab, gather_idx = head_table(width)

        wp = w_qkv.reshape(feat_blk, 3, piece)
        got = [lax.ppermute(wp[:, j, :], COL, perms[j]) for j in range(3)]
        reg = jnp.asarray(regions)[rho]
        wr = []
        for s in range(3):
            acc = jnp.where(reg[0] == s, got[0], got[1])
            acc = jnp.where(reg[2] == s, got[2], acc)
            wr.append(acc)
        wr = jnp.stack(wr, axis=1)
        wg = lax.all_gather(wr, "x", axis=2, tiled=False)
        wg = wg.reshape(feat_blk, 3 * nx * piece)

        tq = tokens.reshape(nx, quarter, feat_blk)
        tq = lax.all_to_all(tq, "x", 0, 0, tiled=True)
        tq = lax.all_gather(tq, "z", axis=0, tiled=False)
        tq = jnp.transpose(tq, (1, 0, 2, 3)).reshape(nc * quarter, feat_blk)

        part = jnp.dot(tq, wg, preferred_element_type=jnp.float32).astype(jnp.bfloat16)
        n_packs = nc // 2
        part = part.reshape(n_packs, 2 * quarter, 3 * nx * piece)
        mine = lax.psum_scatter(part, ROW, scatter_dimension=0, tiled=True)[0]
        mine = mine.reshape(2 * quarter, 3, nx * piece)

        qv = mine[:, 0, :].astype(jnp.float32)
        kv = mine[:, 1, :].astype(jnp.float32)
        sums = jnp.stack([jnp.sum(qv * qv, axis=-1), jnp.sum(kv * kv, axis=-1)], axis=-1)
        sums = lax.psum(sums, "z")
        rs = lax.rsqrt(sums / width + 1e-06)
        qg = lax.dynamic_slice_in_dim(q_gain, z * nx * piece, nx * piece)
        kg = lax.dynamic_slice_in_dim(k_gain, z * nx * piece, nx * piece)
        nq = (qv * rs[:, 0:1] * qg).astype(jnp.bfloat16)
        nk = (kv * rs[:, 1:2] * kg).astype(jnp.bfloat16)
        normed = jnp.stack([nq, nk, mine[:, 2, :]], axis=1)

        normed = normed.reshape(2 * quarter, 3, nx, piece)
        sl = lax.all_to_all(normed, "x", 2, 0, tiled=True)
        sl = sl.reshape(pack_tokens, 3, piece)
        ext = lax.ppermute(sl[:, :, :HEAD_WIDTH], COL, shift_pairs)
        sl = jnp.concatenate([sl, ext], axis=2)

        offs = jnp.asarray(off_tab)[rho]
        heads = jnp.stack(
            [lax.dynamic_slice_in_dim(sl, offs[i], HEAD_WIDTH, axis=2) for i in range(2)], axis=2
        )
        q3 = heads[:, 0]
        k3 = heads[:, 1]
        v3 = heads[:, 2]

        ids = segment_ids[0].reshape(2, nx, quarter).transpose(1, 0, 2).reshape(pack_tokens)
        scores = jnp.einsum("qhd,khd->hqk", q3, k3, preferred_element_type=jnp.float32)
        scores = scores * HEAD_WIDTH ** (-0.5)
        mask = (ids[:, None] == ids[None, :])[None]
        masked = jnp.where(mask, scores, -1e30)
        top = jnp.max(masked, axis=-1, keepdims=True)
        expo = jnp.where(mask, jnp.exp(masked - top), 0.0)
        total = jnp.sum(expo, axis=-1)
        weights = expo.astype(jnp.bfloat16)
        summed = jnp.einsum("hqk,khd->hqd", weights, v3, preferred_element_type=jnp.float32)
        res = (summed / total[..., None]).astype(jnp.bfloat16)

        tpc = pack_tokens // nc
        res = res.reshape(2, nx, 2, quarter // tpc, tpc, HEAD_WIDTH)
        res = jnp.transpose(res, (2, 1, 3, 4, 0, 5)).reshape(nc, tpc, 2, HEAD_WIDTH)
        back = lax.all_to_all(res, COL, 0, 0, tiled=True)
        back = jnp.transpose(back, (0, 2, 1, 3)).reshape(nc * 2, tpc, HEAD_WIDTH)
        out = jnp.take(back, jnp.asarray(gather_idx), axis=0)
        return jnp.transpose(out, (1, 0, 2)).reshape(tpc, width)

    return local


def solution(mesh):
    nr, nc = mesh.devices.shape
    nx = 4
    nz = nc // nx
    m4 = Mesh(mesh.devices.reshape(nr // 2, 2, nx, nz), ("y", "k", "x", "z"))
    return jax.shard_map(
        build_local(nx, nz),
        mesh=m4,
        in_specs=(P(COL, ROW), P(ROW, COL), P(), P(), P(ROW, None)),
        out_specs=P(ROW + COL, None),
        check_vma=False,
    )
```

```python
import numpy as np
import jax
import jax.numpy as jnp
from jax import lax
from jax.sharding import Mesh, PartitionSpec as P

ATTENTION_HEADS = 25
HEAD_WIDTH = 128
ROW = ("y", "k")
COL = ("x", "z")


def shift_gather(v, axis, n, me, dim):
    shape = list(v.shape)
    shape.insert(dim, n)
    out = jnp.zeros(shape, v.dtype)
    out = lax.dynamic_update_index_in_dim(out, v, me, dim)
    for s in range(1, n):
        got = lax.ppermute(v, axis, [(i, (i + s) % n) for i in range(n)])
        out = lax.dynamic_update_index_in_dim(out, got, (me - s) % n, dim)
    return out


def shift_all_to_all(v, axis, n, me):
    out = jnp.zeros_like(v)
    out = lax.dynamic_update_index_in_dim(out, lax.dynamic_index_in_dim(v, me, 0, False), me, 0)
    for s in range(1, n):
        piece = lax.dynamic_index_in_dim(v, (me + s) % n, 0, False)
        got = lax.ppermute(piece, axis, [(i, (i + s) % n) for i in range(n)])
        out = lax.dynamic_update_index_in_dim(out, got, (me - s) % n, 0)
    return out


def butterfly_sum(v, axis, n):
    step = 1
    while step < n:
        v = v + lax.ppermute(v, axis, [(i, i ^ step) for i in range(n)])
        step *= 2
    return v


def build_local(nx, nz):
    nc = nx * nz

    def col_of_rho(rho):
        return (rho % nx) * nz + rho // nx

    perms, regions = [], np.zeros((nc, 3), np.int32)
    for j in range(3):
        pairs = []
        for src in range(nc):
            rho = (3 * src + j) % nc
            regions[rho, j] = (3 * src + j) // nc
            pairs.append((src, col_of_rho(rho)))
        perms.append(pairs)
    assert all(sorted(regions[r]) == [0, 1, 2] for r in range(nc))

    def head_table(width):
        piece = width // nc
        h0 = np.zeros(nc, np.int32)
        off = np.zeros((nc, 2), np.int32)
        owner = []
        for rho in range(nc):
            lo, hi = piece * rho, piece * (rho + 1)
            hs = [h for h in range(ATTENTION_HEADS) if lo <= h * HEAD_WIDTH < hi]
            assert 1 <= len(hs) <= 2
            for slot in range(2):
                o = (hs[0] + slot) * HEAD_WIDTH - lo
                off[rho, slot] = min(o, piece)
            for slot, h in enumerate(hs):
                owner.append((h, col_of_rho(rho), slot))
        owner.sort()
        assert [o[0] for o in owner] == list(range(ATTENTION_HEADS))
        gather = np.array([c * 2 + s for _, c, s in owner], np.int32)
        return off, gather

    shift_pairs = [(col_of_rho(r + 1), col_of_rho(r)) for r in range(nc - 1)]

    def local(tokens, w_qkv, q_gain, k_gain, segment_ids):
        tok_blk, feat_blk = tokens.shape
        width = q_gain.shape[0]
        piece = width // nc
        quarter = tok_blk // nx
        pack_tokens = segment_ids.shape[1]
        x = lax.axis_index("x")
        z = lax.axis_index("z")
        rho = z * nx + x
        off_tab, gather_idx = head_table(width)

        wp = w_qkv.reshape(feat_blk, 3, piece)
        got = [lax.ppermute(wp[:, j, :], COL, perms[j]) for j in range(3)]
        reg = jnp.asarray(regions)[rho]
        wr = []
        for s in range(3):
            acc = jnp.where(reg[0] == s, got[0], got[1])
            acc = jnp.where(reg[2] == s, got[2], acc)
            wr.append(acc)
        wr = jnp.stack(wr, axis=1)
        wg = shift_gather(wr, "x", nx, x, 2)
        wg = wg.reshape(feat_blk, 3 * nx * piece)

        tq = tokens.reshape(nx, quarter, feat_blk)
        tq = shift_all_to_all(tq, "x", nx, x)
        tq = shift_gather(tq, "z", nz, z, 1)
        n_packs = nc // 2
        tq = tq.reshape(n_packs, 2 * quarter, feat_blk)

        part = jnp.einsum("ptf,fc->ptc", tq, wg, preferred_element_type=jnp.float32)
        part = part.astype(jnp.bfloat16)
        mine = lax.psum_scatter(part, ROW, scatter_dimension=0, tiled=True)[0]
        mine = mine.reshape(2 * quarter, 3, nx * piece)

        qv = mine[:, 0, :].astype(jnp.float32)
        kv = mine[:, 1, :].astype(jnp.float32)
        sums = jnp.stack([jnp.sum(qv * qv, axis=-1), jnp.sum(kv * kv, axis=-1)], axis=-1)
        sums = butterfly_sum(sums, "z", nz)
        rs = lax.rsqrt(sums / width + 1e-06)
        qg = lax.dynamic_slice_in_dim(q_gain, z * nx * piece, nx * piece)
        kg = lax.dynamic_slice_in_dim(k_gain, z * nx * piece, nx * piece)
        nq = (qv * rs[:, 0:1] * qg).astype(jnp.bfloat16)
        nk = (kv * rs[:, 1:2] * kg).astype(jnp.bfloat16)
        normed = jnp.stack([nq, nk, mine[:, 2, :]], axis=1)

        normed = normed.reshape(2 * quarter, 3, nx, piece)
        sl = lax.all_to_all(normed, "x", 2, 0, tiled=True)
        sl = sl.reshape(pack_tokens, 3, piece)
        ext = lax.ppermute(sl[:, :, :HEAD_WIDTH], COL, shift_pairs)
        sl = jnp.concatenate([sl, ext], axis=2)

        offs = jnp.asarray(off_tab)[rho]
        heads = jnp.stack(
            [lax.dynamic_slice_in_dim(sl, offs[i], HEAD_WIDTH, axis=2) for i in range(2)], axis=2
        )
        q3 = heads[:, 0]
        k3 = heads[:, 1]
        v3 = heads[:, 2]

        ids = segment_ids[0].reshape(2, nx, quarter).transpose(1, 0, 2).reshape(pack_tokens)
        scores = jnp.einsum("qhd,khd->hqk", q3, k3, preferred_element_type=jnp.float32)
        scores = scores * HEAD_WIDTH ** (-0.5)
        mask = (ids[:, None] == ids[None, :])[None]
        masked = jnp.where(mask, scores, -1e30)
        top = jnp.max(masked, axis=-1, keepdims=True)
        expo = jnp.where(mask, jnp.exp(masked - top), 0.0)
        total = jnp.sum(expo, axis=-1)
        weights = expo.astype(jnp.bfloat16)
        summed = jnp.einsum("hqk,khd->hqd", weights, v3, preferred_element_type=jnp.float32)
        res = (summed / total[..., None]).astype(jnp.bfloat16)

        tpc = pack_tokens // nc
        res = res.reshape(2, nx, 2, quarter // tpc, tpc, HEAD_WIDTH)
        res = jnp.transpose(res, (2, 1, 3, 4, 0, 5)).reshape(nc, tpc, 2, HEAD_WIDTH)
        back = lax.all_to_all(res, COL, 0, 0, tiled=True)
        back = jnp.transpose(back, (0, 2, 1, 3)).reshape(nc * 2, tpc, HEAD_WIDTH)
        out = jnp.take(back, jnp.asarray(gather_idx), axis=0)
        return jnp.transpose(out, (1, 0, 2)).reshape(tpc, width)

    return local


def solution(mesh):
    nr, nc = mesh.devices.shape
    nx = 4
    nz = nc // nx
    m4 = Mesh(mesh.devices.reshape(nr // 2, 2, nx, nz), ("y", "k", "x", "z"))
    return jax.shard_map(
        build_local(nx, nz),
        mesh=m4,
        in_specs=(P(COL, ROW), P(ROW, COL), P(), P(), P(ROW, None)),
        out_specs=P(ROW + COL, None),
        check_vma=False,
    )
```

```python
import numpy as np
import jax
import jax.numpy as jnp
from jax import lax
from jax.sharding import Mesh, PartitionSpec as P

ATTENTION_HEADS = 25
HEAD_WIDTH = 128
ROW = ("y", "k")
COL = ("x", "z")


def place(pieces, me, n, dim):
    outs = []
    for j in range(n):
        acc = pieces[0]
        for s in range(1, n):
            acc = jnp.where((me - s) % n == j, pieces[s], acc)
        outs.append(acc)
    return jnp.stack(outs, dim)


def shift_gather(v, axis, n, me, dim):
    pieces = [v] + [lax.ppermute(v, axis, [(i, (i + s) % n) for i in range(n)]) for s in range(1, n)]
    return place(pieces, me, n, dim)


def shift_all_to_all(v, axis, n, me):
    pieces = [lax.dynamic_index_in_dim(v, me, 0, False)]
    for s in range(1, n):
        piece = lax.dynamic_index_in_dim(v, (me + s) % n, 0, False)
        pieces.append(lax.ppermute(piece, axis, [(i, (i + s) % n) for i in range(n)]))
    return place(pieces, me, n, 0)


def butterfly_sum(v, axis, n):
    step = 1
    while step < n:
        v = v + lax.ppermute(v, axis, [(i, i ^ step) for i in range(n)])
        step *= 2
    return v


def build_local(nx, nz):
    nc = nx * nz

    def col_of_rho(rho):
        return (rho % nx) * nz + rho // nx

    perms, regions = [], np.zeros((nc, 3), np.int32)
    for j in range(3):
        pairs = []
        for src in range(nc):
            rho = (3 * src + j) % nc
            regions[rho, j] = (3 * src + j) // nc
            pairs.append((src, col_of_rho(rho)))
        perms.append(pairs)
    assert all(sorted(regions[r]) == [0, 1, 2] for r in range(nc))

    def head_table(width):
        piece = width // nc
        h0 = np.zeros(nc, np.int32)
        off = np.zeros((nc, 2), np.int32)
        owner = []
        for rho in range(nc):
            lo, hi = piece * rho, piece * (rho + 1)
            hs = [h for h in range(ATTENTION_HEADS) if lo <= h * HEAD_WIDTH < hi]
            assert 1 <= len(hs) <= 2
            for slot in range(2):
                o = (hs[0] + slot) * HEAD_WIDTH - lo
                off[rho, slot] = min(o, piece)
            for slot, h in enumerate(hs):
                owner.append((h, col_of_rho(rho), slot))
        owner.sort()
        assert [o[0] for o in owner] == list(range(ATTENTION_HEADS))
        gather = np.array([c * 2 + s for _, c, s in owner], np.int32)
        return off, gather

    shift_pairs = [(col_of_rho(r + 1), col_of_rho(r)) for r in range(nc - 1)]

    def local(tokens, w_qkv, q_gain, k_gain, segment_ids):
        tok_blk, feat_blk = tokens.shape
        width = q_gain.shape[0]
        piece = width // nc
        quarter = tok_blk // nx
        pack_tokens = segment_ids.shape[1]
        x = lax.axis_index("x")
        z = lax.axis_index("z")
        rho = z * nx + x
        off_tab, gather_idx = head_table(width)

        wp = w_qkv.reshape(feat_blk, 3, piece)
        got = [lax.ppermute(wp[:, j, :], COL, perms[j]) for j in range(3)]
        reg = jnp.asarray(regions)[rho]
        wr = []
        for s in range(3):
            acc = jnp.where(reg[0] == s, got[0], got[1])
            acc = jnp.where(reg[2] == s, got[2], acc)
            wr.append(acc)
        wr = jnp.stack(wr, axis=1)
        wg = shift_gather(wr, "x", nx, x, 2)
        wg = wg.reshape(feat_blk, 3 * nx * piece)

        tq = tokens.reshape(nx, quarter, feat_blk)
        tq = shift_all_to_all(tq, "x", nx, x)
        n_packs = nc // 2
        half = quarter // 2
        qg = lax.dynamic_slice_in_dim(q_gain, z * nx * piece, nx * piece)
        kg = lax.dynamic_slice_in_dim(k_gain, z * nx * piece, nx * piece)
        done = []
        for tc in range(2):
            th = tq[:, tc * half:(tc + 1) * half]
            th = shift_gather(th, "z", nz, z, 1)
            th = th.reshape(n_packs, 2 * half, feat_blk)
            part = jnp.einsum("ptf,fc->ptc", th, wg, preferred_element_type=jnp.float32)
            part = part.astype(jnp.bfloat16)
            mine = lax.psum_scatter(part, ROW, scatter_dimension=0, tiled=True)[0]
            mine = mine.reshape(2 * half, 3, nx * piece)

            qv = mine[:, 0, :].astype(jnp.float32)
            kv = mine[:, 1, :].astype(jnp.float32)
            sums = jnp.stack([jnp.sum(qv * qv, axis=-1), jnp.sum(kv * kv, axis=-1)], axis=-1)
            sums = butterfly_sum(sums, "z", nz)
            rs = lax.rsqrt(sums / width + 1e-06)
            nq = (qv * rs[:, 0:1] * qg).astype(jnp.bfloat16)
            nk = (kv * rs[:, 1:2] * kg).astype(jnp.bfloat16)
            normed = jnp.stack([nq, nk, mine[:, 2, :]], axis=1)

            normed = normed.reshape(2 * half, 3, nx, piece)
            got = lax.all_to_all(normed, "x", 2, 0, tiled=True)
            done.append(got.reshape(nx, 2, half, 3, piece))
        sl = jnp.stack(done, axis=2).reshape(pack_tokens, 3, piece)
        ext = lax.ppermute(sl[:, :, :HEAD_WIDTH], COL, shift_pairs)
        sl = jnp.concatenate([sl, ext], axis=2)

        offs = jnp.asarray(off_tab)[rho]
        heads = jnp.stack(
            [lax.dynamic_slice_in_dim(sl, offs[i], HEAD_WIDTH, axis=2) for i in range(2)], axis=2
        )
        q3 = heads[:, 0]
        k3 = heads[:, 1]
        v3 = heads[:, 2]

        ids = segment_ids[0].reshape(2, nx, quarter).transpose(1, 0, 2).reshape(pack_tokens)
        scores = jnp.einsum("qhd,khd->hqk", q3, k3, preferred_element_type=jnp.float32)
        scores = scores * HEAD_WIDTH ** (-0.5)
        mask = (ids[:, None] == ids[None, :])[None]
        masked = jnp.where(mask, scores, -1e30)
        top = jnp.max(masked, axis=-1, keepdims=True)
        expo = jnp.where(mask, jnp.exp(masked - top), 0.0)
        total = jnp.sum(expo, axis=-1)
        weights = expo.astype(jnp.bfloat16)
        summed = jnp.einsum("hqk,khd->hqd", weights, v3, preferred_element_type=jnp.float32)
        res = (summed / total[..., None]).astype(jnp.bfloat16)

        tpc = pack_tokens // nc
        res = res.reshape(2, nx, 2, quarter // tpc, tpc, HEAD_WIDTH)
        res = jnp.transpose(res, (2, 1, 3, 4, 0, 5)).reshape(nc, tpc, 2, HEAD_WIDTH)
        back = lax.all_to_all(res, COL, 0, 0, tiled=True)
        back = jnp.transpose(back, (0, 2, 1, 3)).reshape(nc * 2, tpc, HEAD_WIDTH)
        out = jnp.take(back, jnp.asarray(gather_idx), axis=0)
        return jnp.transpose(out, (1, 0, 2)).reshape(tpc, width)

    return local


def solution(mesh):
    nr, nc = mesh.devices.shape
    nx = 4
    nz = nc // nx
    m4 = Mesh(mesh.devices.reshape(nr // 2, 2, nx, nz), ("y", "k", "x", "z"))
    return jax.shard_map(
        build_local(nx, nz),
        mesh=m4,
        in_specs=(P(COL, ROW), P(ROW, COL), P(), P(), P(ROW, None)),
        out_specs=P(ROW + COL, None),
        check_vma=False,
    )
```

```python
import numpy as np
import jax
import jax.numpy as jnp
from jax import lax
from jax.sharding import Mesh, PartitionSpec as P

ATTENTION_HEADS = 25
HEAD_WIDTH = 128
ROW = ("y", "k")
COL = ("x", "z")


def place(pieces, me, n, dim):
    outs = []
    for j in range(n):
        acc = pieces[0]
        for s in range(1, n):
            acc = jnp.where((me - s) % n == j, pieces[s], acc)
        outs.append(acc)
    return jnp.stack(outs, dim)


def shift_gather(v, axis, n, me, dim):
    pieces = [v] + [lax.ppermute(v, axis, [(i, (i + s) % n) for i in range(n)]) for s in range(1, n)]
    return place(pieces, me, n, dim)


def shift_all_to_all(v, axis, n, me):
    pieces = [lax.dynamic_index_in_dim(v, me, 0, False)]
    for s in range(1, n):
        piece = lax.dynamic_index_in_dim(v, (me + s) % n, 0, False)
        pieces.append(lax.ppermute(piece, axis, [(i, (i + s) % n) for i in range(n)]))
    return place(pieces, me, n, 0)


def butterfly_sum(v, axis, n):
    step = 1
    while step < n:
        v = v + lax.ppermute(v, axis, [(i, i ^ step) for i in range(n)])
        step *= 2
    return v


def build_local(nx, nz):
    nc = nx * nz

    def col_of_rho(rho):
        return (rho % nx) * nz + rho // nx

    perms, regions = [], np.zeros((nc, 3), np.int32)
    for j in range(3):
        pairs = []
        for src in range(nc):
            rho = (3 * src + j) % nc
            regions[rho, j] = (3 * src + j) // nc
            pairs.append((src, col_of_rho(rho)))
        perms.append(pairs)
    assert all(sorted(regions[r]) == [0, 1, 2] for r in range(nc))

    def head_table(width):
        piece = width // nc
        off = np.zeros((nc, 2), np.int32)
        owner = []
        for rho in range(nc):
            lo, hi = piece * rho, piece * (rho + 1)
            hs = [h for h in range(ATTENTION_HEADS) if lo <= h * HEAD_WIDTH < hi]
            assert 1 <= len(hs) <= 2
            for slot in range(2):
                o = (hs[0] + slot) * HEAD_WIDTH - lo
                off[rho, slot] = min(o, piece)
            for slot, h in enumerate(hs):
                owner.append((h, col_of_rho(rho), slot))
        owner.sort()
        assert [o[0] for o in owner] == list(range(ATTENTION_HEADS))
        gather = np.array([c * 2 + s for _, c, s in owner], np.int32)
        return off, gather

    shift_pairs = [(col_of_rho(r + 1), col_of_rho(r)) for r in range(nc - 1)]

    def body(tokens, w_qkv, q_gain, k_gain, segment_ids):
        tok_blk, feat_blk = tokens.shape
        width = q_gain.shape[0]
        piece = width // nc
        quarter = tok_blk // nx
        pack_tokens = segment_ids.shape[1]
        x = lax.axis_index("x")
        z = lax.axis_index("z")
        rho = z * nx + x
        off_tab, gather_idx = head_table(width)

        wp = w_qkv.reshape(feat_blk, 3, piece)
        got = [lax.ppermute(wp[:, j, :], COL, perms[j]) for j in range(3)]
        reg = jnp.asarray(regions)[rho]
        wr = []
        for s in range(3):
            acc = jnp.where(reg[0] == s, got[0], got[1])
            acc = jnp.where(reg[2] == s, got[2], acc)
            wr.append(acc)
        wr = jnp.stack(wr, axis=1)
        wg = shift_gather(wr, "x", nx, x, 2)
        wg = wg.reshape(feat_blk, 3 * nx * piece)

        tq = tokens.reshape(nx, quarter, feat_blk)
        tq = shift_all_to_all(tq, "x", nx, x)
        n_packs = nc // 2
        half = quarter // 2
        qg = lax.dynamic_slice_in_dim(q_gain, z * nx * piece, nx * piece)
        kg = lax.dynamic_slice_in_dim(k_gain, z * nx * piece, nx * piece)
        done = []
        for tc in range(2):
          th = tq[:, tc * half:(tc + 1) * half]
          th = shift_gather(th, "z", nz, z, 1)
          th = th.reshape(n_packs, 2 * half, feat_blk)
          part = jnp.einsum("ptf,fc->ptc", th, wg, preferred_element_type=jnp.float32)
          part = part.astype(jnp.bfloat16)
          mine = lax.psum_scatter(part, ROW, scatter_dimension=0, tiled=True)[0]
          mine = mine.reshape(2 * half, 3, nx * piece)
          mine, qgc, kgc, xc = lax.optimization_barrier((mine, qg, kg, x))

          qv = mine[:, 0, :].astype(jnp.float32)
          kv = mine[:, 1, :].astype(jnp.float32)
          sums = jnp.stack([jnp.sum(qv * qv, axis=-1), jnp.sum(kv * kv, axis=-1)], axis=-1)
          sums = butterfly_sum(sums, "z", nz)
          rs = lax.rsqrt(sums / width + 1e-06)
          nq = (qv * rs[:, 0:1] * qgc).astype(jnp.bfloat16)
          nk = (kv * rs[:, 1:2] * kgc).astype(jnp.bfloat16)
          normed = jnp.stack([nq, nk, mine[:, 2, :]], axis=1)

          normed = normed.reshape(2 * half, 3, nx, piece)
          got = shift_all_to_all(jnp.moveaxis(normed, 2, 0), "x", nx, xc)
          done.append(got.reshape(nx, 2, half, 3, piece))
        sl = jnp.stack(done, axis=2).reshape(pack_tokens, 3, piece)
        ext = lax.ppermute(sl[:, :, :HEAD_WIDTH], COL, shift_pairs)
        sl = jnp.concatenate([sl, ext], axis=2)

        offs = jnp.asarray(off_tab)[rho]
        heads = jnp.stack(
            [lax.dynamic_slice_in_dim(sl, offs[i], HEAD_WIDTH, axis=2) for i in range(2)], axis=2
        )
        q3 = heads[:, 0]
        k3 = heads[:, 1]
        v3 = heads[:, 2]

        ids = segment_ids[0].reshape(2, nx, quarter).transpose(1, 0, 2).reshape(pack_tokens)
        scores = jnp.einsum("qhd,khd->hqk", q3, k3, preferred_element_type=jnp.float32)
        scores = scores * HEAD_WIDTH ** (-0.5)
        mask = (ids[:, None] == ids[None, :])[None]
        masked = jnp.where(mask, scores, -1e30)
        top = jnp.max(masked, axis=-1, keepdims=True)
        expo = jnp.where(mask, jnp.exp(masked - top), 0.0)
        total = jnp.sum(expo, axis=-1)
        weights = expo.astype(jnp.bfloat16)
        summed = jnp.einsum("hqk,khd->hqd", weights, v3, preferred_element_type=jnp.float32)
        res = (summed / total[..., None]).astype(jnp.bfloat16)

        tpc = pack_tokens // nc
        res = res.reshape(2, nx, 2, quarter // tpc, tpc, HEAD_WIDTH)
        res = jnp.transpose(res, (2, 1, 3, 4, 0, 5)).reshape(nc, tpc, 2, HEAD_WIDTH)
        back = lax.all_to_all(res, COL, 0, 0, tiled=True)
        back = jnp.transpose(back, (0, 2, 1, 3)).reshape(nc * 2, tpc, HEAD_WIDTH)
        out = jnp.take(back, jnp.asarray(gather_idx), axis=0)
        return jnp.transpose(out, (1, 0, 2)).reshape(tpc, width)

    return body


def solution(mesh):
    nr, nc = mesh.devices.shape
    nx = 4
    nz = nc // nx
    m4 = Mesh(mesh.devices.reshape(nr // 2, 2, nx, nz), ("y", "k", "x", "z"))
    return jax.shard_map(
        build_local(nx, nz),
        mesh=m4,
        in_specs=(P(COL, ROW), P(ROW, COL), P(), P(), P(ROW, None)),
        out_specs=P(ROW + COL, None),
        check_vma=False,
    )
```

```python
import numpy as np
import jax
import jax.numpy as jnp
from jax import lax
from jax.sharding import Mesh, PartitionSpec as P

ATTENTION_HEADS = 25
HEAD_WIDTH = 128
ROW = ("y", "k")
COL = ("x", "z")


def place(pieces, me, n, dim):
    outs = []
    for j in range(n):
        acc = pieces[0]
        for s in range(1, n):
            acc = jnp.where((me - s) % n == j, pieces[s], acc)
        outs.append(acc)
    return jnp.stack(outs, dim)


def shift_gather(v, axis, n, me, dim):
    pieces = [v] + [lax.ppermute(v, axis, [(i, (i + s) % n) for i in range(n)]) for s in range(1, n)]
    return place(pieces, me, n, dim)


def shift_all_to_all(v, axis, n, me):
    pieces = [lax.dynamic_index_in_dim(v, me, 0, False)]
    for s in range(1, n):
        piece = lax.dynamic_index_in_dim(v, (me + s) % n, 0, False)
        pieces.append(lax.ppermute(piece, axis, [(i, (i + s) % n) for i in range(n)]))
    return place(pieces, me, n, 0)


def butterfly_sum(v, axis, n):
    step = 1
    while step < n:
        v = v + lax.ppermute(v, axis, [(i, i ^ step) for i in range(n)])
        step *= 2
    return v


def build_local(nx, nz):
    nc = nx * nz

    def col_of_rho(rho):
        return (rho % nx) * nz + rho // nx

    perms, regions = [], np.zeros((nc, 3), np.int32)
    for j in range(3):
        pairs = []
        for src in range(nc):
            rho = (3 * src + j) % nc
            regions[rho, j] = (3 * src + j) // nc
            pairs.append((src, col_of_rho(rho)))
        perms.append(pairs)
    assert all(sorted(regions[r]) == [0, 1, 2] for r in range(nc))

    def head_table(width):
        piece = width // nc
        off = np.zeros((nc, 2), np.int32)
        owner = []
        for rho in range(nc):
            lo, hi = piece * rho, piece * (rho + 1)
            hs = [h for h in range(ATTENTION_HEADS) if lo <= h * HEAD_WIDTH < hi]
            assert 1 <= len(hs) <= 2
            for slot in range(2):
                o = (hs[0] + slot) * HEAD_WIDTH - lo
                off[rho, slot] = min(o, piece)
            for slot, h in enumerate(hs):
                owner.append((h, col_of_rho(rho), slot))
        owner.sort()
        assert [o[0] for o in owner] == list(range(ATTENTION_HEADS))
        gather = np.array([c * 2 + s for _, c, s in owner], np.int32)
        return off, gather

    shift_pairs = [(col_of_rho(r + 1), col_of_rho(r)) for r in range(nc - 1)]

    def body(tokens, w_qkv, q_gain, k_gain, segment_ids):
        tok_blk, feat_blk = tokens.shape
        width = q_gain.shape[0]
        piece = width // nc
        quarter = tok_blk // nx
        pack_tokens = segment_ids.shape[1]
        x = lax.axis_index("x")
        z = lax.axis_index("z")
        rho = z * nx + x
        off_tab, gather_idx = head_table(width)

        wp = w_qkv.reshape(feat_blk, 3, piece)
        got = [lax.ppermute(wp[:, j, :], COL, perms[j]) for j in range(3)]
        reg = jnp.asarray(regions)[rho]
        wr = []
        for s in range(3):
            acc = jnp.where(reg[0] == s, got[0], got[1])
            acc = jnp.where(reg[2] == s, got[2], acc)
            wr.append(acc)
        wr = jnp.stack(wr, axis=1)
        wg = shift_gather(wr, "x", nx, x, 2)
        wg = wg.reshape(feat_blk, 3 * nx * piece)

        tq = tokens.reshape(nx, quarter, feat_blk)
        tq = shift_all_to_all(tq, "x", nx, x)
        n_packs = nc // 2
        half = quarter // 2
        qg = lax.dynamic_slice_in_dim(q_gain, z * nx * piece, nx * piece)
        kg = lax.dynamic_slice_in_dim(k_gain, z * nx * piece, nx * piece)
        done = []
        for tc in range(2):
          th = tq[:, tc * half:(tc + 1) * half]
          th = shift_gather(th, "z", nz, z, 1)
          th = th.reshape(n_packs, 2 * half, feat_blk)
          part = jnp.einsum("ptf,fc->ptc", th, wg, preferred_element_type=jnp.float32)
          part = part.astype(jnp.bfloat16)
          mine = lax.psum_scatter(part, ROW, scatter_dimension=0, tiled=True)[0]
          mine = mine.reshape(2 * half, 3, nx * piece)
          mine, qgc, kgc, xc = lax.optimization_barrier((mine, qg, kg, x))

          qv = mine[:, 0, :].astype(jnp.float32)
          kv = mine[:, 1, :].astype(jnp.float32)
          sums = jnp.stack([jnp.sum(qv * qv, axis=-1), jnp.sum(kv * kv, axis=-1)], axis=-1)
          sums = butterfly_sum(sums, "z", nz)
          rs = lax.rsqrt(sums / width + 1e-06)
          nq = (qv * rs[:, 0:1] * qgc).astype(jnp.bfloat16)
          nk = (kv * rs[:, 1:2] * kgc).astype(jnp.bfloat16)
          normed = jnp.stack([nq, nk, mine[:, 2, :]], axis=1)

          normed = normed.reshape(2 * half, 3, nx, piece)
          got = shift_all_to_all(jnp.moveaxis(normed, 2, 0), "x", nx, xc)
          ext = lax.ppermute(got[..., :HEAD_WIDTH], COL, shift_pairs)
          got = jnp.concatenate([got, ext], axis=-1)
          done.append(got.reshape(nx, 2, half, 3, piece + HEAD_WIDTH))
        sl = jnp.stack(done, axis=2).reshape(pack_tokens, 3, piece + HEAD_WIDTH)

        offs = jnp.asarray(off_tab)[rho]
        heads = jnp.stack(
            [lax.dynamic_slice_in_dim(sl, offs[i], HEAD_WIDTH, axis=2) for i in range(2)], axis=2
        )
        q3 = heads[:, 0]
        k3 = heads[:, 1]
        v3 = heads[:, 2]

        ids = segment_ids[0].reshape(2, nx, quarter).transpose(1, 0, 2).reshape(pack_tokens)
        scores = jnp.einsum("qhd,khd->hqk", q3, k3, preferred_element_type=jnp.float32)
        scores = scores * HEAD_WIDTH ** (-0.5)
        mask = (ids[:, None] == ids[None, :])[None]
        masked = jnp.where(mask, scores, -1e30)
        top = jnp.max(masked, axis=-1, keepdims=True)
        expo = jnp.where(mask, jnp.exp(masked - top), 0.0)
        total = jnp.sum(expo, axis=-1)
        weights = expo.astype(jnp.bfloat16)
        summed = jnp.einsum("hqk,khd->hqd", weights, v3, preferred_element_type=jnp.float32)
        res = (summed / total[..., None]).astype(jnp.bfloat16)

        tpc = pack_tokens // nc
        res = res.reshape(2, nx, 2, quarter // tpc, tpc, HEAD_WIDTH)
        res = jnp.transpose(res, (2, 1, 3, 4, 0, 5)).reshape(nc, tpc, 2, HEAD_WIDTH)
        back = lax.all_to_all(res, COL, 0, 0, tiled=True)
        back = jnp.transpose(back, (0, 2, 1, 3)).reshape(nc * 2, tpc, HEAD_WIDTH)
        out = jnp.take(back, jnp.asarray(gather_idx), axis=0)
        return jnp.transpose(out, (1, 0, 2)).reshape(tpc, width)

    return body


def solution(mesh):
    nr, nc = mesh.devices.shape
    nx = 4
    nz = nc // nx
    m4 = Mesh(mesh.devices.reshape(nr // 2, 2, nx, nz), ("y", "k", "x", "z"))
    return jax.shard_map(
        build_local(nx, nz),
        mesh=m4,
        in_specs=(P(COL, ROW), P(ROW, COL), P(), P(), P(ROW, None)),
        out_specs=P(ROW + COL, None),
        check_vma=False,
    )
```

```python
import numpy as np
import jax
import jax.numpy as jnp
from jax import lax
from jax.sharding import Mesh, PartitionSpec as P

ATTENTION_HEADS = 25
HEAD_WIDTH = 128
ROW = ("y", "k")
COL = ("x", "z")


def place(pieces, me, n, dim):
    outs = []
    for j in range(n):
        acc = pieces[0]
        for s in range(1, n):
            acc = jnp.where((me - s) % n == j, pieces[s], acc)
        outs.append(acc)
    return jnp.stack(outs, dim)


def shift_gather(v, axis, n, me, dim):
    pieces = [v] + [lax.ppermute(v, axis, [(i, (i + s) % n) for i in range(n)]) for s in range(1, n)]
    return place(pieces, me, n, dim)


def shift_all_to_all(v, axis, n, me):
    pieces = [lax.dynamic_index_in_dim(v, me, 0, False)]
    for s in range(1, n):
        piece = lax.dynamic_index_in_dim(v, (me + s) % n, 0, False)
        pieces.append(lax.ppermute(piece, axis, [(i, (i + s) % n) for i in range(n)]))
    return place(pieces, me, n, 0)


def butterfly_sum(v, axis, n, me):
    pieces = [v] + [lax.ppermute(v, axis, [(i, (i + s) % n) for i in range(n)]) for s in range(1, n)]
    ordered = place(pieces, me, n, 0)
    total = ordered[0]
    for j in range(1, n):
        total = total + ordered[j]
    return total


def build_local(nx, nz):
    nc = nx * nz

    def col_of_rho(rho):
        return (rho % nx) * nz + rho // nx

    perms, regions = [], np.zeros((nc, 3), np.int32)
    for j in range(3):
        pairs = []
        for src in range(nc):
            rho = (3 * src + j) % nc
            regions[rho, j] = (3 * src + j) // nc
            pairs.append((src, col_of_rho(rho)))
        perms.append(pairs)
    assert all(sorted(regions[r]) == [0, 1, 2] for r in range(nc))

    def head_table(width):
        piece = width // nc
        off = np.zeros((nc, 2), np.int32)
        owner = []
        for rho in range(nc):
            lo, hi = piece * rho, piece * (rho + 1)
            hs = [h for h in range(ATTENTION_HEADS) if lo <= h * HEAD_WIDTH < hi]
            assert 1 <= len(hs) <= 2
            for slot in range(2):
                o = (hs[0] + slot) * HEAD_WIDTH - lo
                off[rho, slot] = min(o, piece)
            for slot, h in enumerate(hs):
                owner.append((h, col_of_rho(rho), slot))
        owner.sort()
        assert [o[0] for o in owner] == list(range(ATTENTION_HEADS))
        gather = np.array([c * 2 + s for _, c, s in owner], np.int32)
        return off, gather

    shift_pairs = [(col_of_rho(r + 1), col_of_rho(r)) for r in range(nc - 1)]

    def body(tokens, w_qkv, q_gain, k_gain, segment_ids):
        tok_blk, feat_blk = tokens.shape
        width = q_gain.shape[0]
        piece = width // nc
        quarter = tok_blk // nx
        pack_tokens = segment_ids.shape[1]
        x = lax.axis_index("x")
        z = lax.axis_index("z")
        rho = z * nx + x
        off_tab, gather_idx = head_table(width)

        wp = w_qkv.reshape(feat_blk, 3, piece)
        got = [lax.ppermute(wp[:, j, :], COL, perms[j]) for j in range(3)]
        reg = jnp.asarray(regions)[rho]
        wr = []
        for s in range(3):
            acc = jnp.where(reg[0] == s, got[0], got[1])
            acc = jnp.where(reg[2] == s, got[2], acc)
            wr.append(acc)
        wr = jnp.stack(wr, axis=0)
        pieces = [wr] + [lax.ppermute(wr, "x", [(i, (i + s) % nx) for i in range(nx)]) for s in range(1, nx)]
        cols = []
        for reg_i in range(3):
            for j in range(nx):
                acc = pieces[0][reg_i]
                for s in range(1, nx):
                    acc = jnp.where((x - s) % nx == j, pieces[s][reg_i], acc)
                cols.append(acc)
        wg = jnp.concatenate(cols, axis=1)

        tq = tokens.reshape(nx, quarter, feat_blk)
        tq = shift_all_to_all(tq, "x", nx, x)
        n_packs = nc // 2
        half = quarter // 2
        qg = lax.dynamic_slice_in_dim(q_gain, z * nx * piece, nx * piece)
        kg = lax.dynamic_slice_in_dim(k_gain, z * nx * piece, nx * piece)
        done = []
        for tc in range(2):
          th = tq[:, tc * half:(tc + 1) * half]
          th = shift_gather(th, "z", nz, z, 1)
          th = th.reshape(n_packs, 2 * half, feat_blk)
          part = jnp.einsum("ptf,fc->ptc", th, wg, preferred_element_type=jnp.float32)
          part = part.astype(jnp.bfloat16)
          mine = lax.psum_scatter(part, ROW, scatter_dimension=0, tiled=True)[0]
          mine = mine.reshape(2 * half, 3, nx * piece)
          mine, qgc, kgc, xc, zc = lax.optimization_barrier((mine, qg, kg, x, z))

          qv = mine[:, 0, :].astype(jnp.float32)
          kv = mine[:, 1, :].astype(jnp.float32)
          sums = jnp.stack([jnp.sum(qv * qv, axis=-1), jnp.sum(kv * kv, axis=-1)], axis=-1)
          sums = butterfly_sum(sums, "z", nz, zc)
          rs = lax.rsqrt(sums / width + 1e-06)
          nq = (qv * rs[:, 0:1] * qgc).astype(jnp.bfloat16)
          nk = (kv * rs[:, 1:2] * kgc).astype(jnp.bfloat16)
          normed = jnp.stack([nq, nk, mine[:, 2, :]], axis=1)

          normed = normed.reshape(2 * half, 3, nx, piece)
          got = shift_all_to_all(jnp.moveaxis(normed, 2, 0), "x", nx, xc)
          ext = lax.ppermute(got[..., :HEAD_WIDTH], COL, shift_pairs)
          got = jnp.concatenate([got, ext], axis=-1)
          done.append(got.reshape(nx, 2, half, 3, piece + HEAD_WIDTH))
        sl = jnp.stack(done, axis=2).reshape(pack_tokens, 3, piece + HEAD_WIDTH)

        offs = jnp.asarray(off_tab)[rho]
        heads = jnp.stack(
            [lax.dynamic_slice_in_dim(sl, offs[i], HEAD_WIDTH, axis=2) for i in range(2)], axis=2
        )
        q3 = heads[:, 0]
        k3 = heads[:, 1]
        v3 = heads[:, 2]

        ids = segment_ids[0].reshape(2, nx, quarter).transpose(1, 0, 2).reshape(pack_tokens)
        scores = jnp.einsum("qhd,khd->hqk", q3, k3, preferred_element_type=jnp.float32)
        scores = scores * HEAD_WIDTH ** (-0.5)
        mask = (ids[:, None] == ids[None, :])[None]
        masked = jnp.where(mask, scores, -1e30)
        top = jnp.max(masked, axis=-1, keepdims=True)
        expo = jnp.where(mask, jnp.exp(masked - top), 0.0)
        total = jnp.sum(expo, axis=-1)
        weights = expo.astype(jnp.bfloat16)
        summed = jnp.einsum("hqk,khd->hqd", weights, v3, preferred_element_type=jnp.float32)
        res = (summed / total[..., None]).astype(jnp.bfloat16)

        tpc = pack_tokens // nc
        res = res.reshape(2, nx, 2, quarter // tpc, tpc, HEAD_WIDTH)
        res = jnp.transpose(res, (2, 1, 3, 4, 0, 5)).reshape(nc, tpc, 2, HEAD_WIDTH)
        back = lax.all_to_all(res, COL, 0, 0, tiled=True)
        back = jnp.transpose(back, (0, 2, 1, 3)).reshape(nc * 2, tpc, HEAD_WIDTH)
        out = jnp.take(back, jnp.asarray(gather_idx), axis=0)
        return jnp.transpose(out, (1, 0, 2)).reshape(tpc, width)

    return body


def solution(mesh):
    nr, nc = mesh.devices.shape
    nx = 4
    nz = nc // nx
    m4 = Mesh(mesh.devices.reshape(nr // 2, 2, nx, nz), ("y", "k", "x", "z"))
    return jax.shard_map(
        build_local(nx, nz),
        mesh=m4,
        in_specs=(P(COL, ROW), P(ROW, COL), P(), P(), P(ROW, None)),
        out_specs=P(ROW + COL, None),
        check_vma=False,
    )
```

```python
import numpy as np
import jax
import jax.numpy as jnp
from jax import lax
from jax.sharding import Mesh, PartitionSpec as P

ATTENTION_HEADS = 25
HEAD_WIDTH = 128
ROW = ("y", "k")
COL = ("x", "z")


def place(pieces, me, n, dim):
    outs = []
    for j in range(n):
        acc = pieces[0]
        for s in range(1, n):
            acc = jnp.where((me - s) % n == j, pieces[s], acc)
        outs.append(acc)
    return jnp.stack(outs, dim)


def shift_gather(v, axis, n, me, dim):
    pieces = [v] + [lax.ppermute(v, axis, [(i, (i + s) % n) for i in range(n)]) for s in range(1, n)]
    return place(pieces, me, n, dim)


def shift_all_to_all(v, axis, n, me):
    pieces = [lax.dynamic_index_in_dim(v, me, 0, False)]
    for s in range(1, n):
        piece = lax.dynamic_index_in_dim(v, (me + s) % n, 0, False)
        pieces.append(lax.ppermute(piece, axis, [(i, (i + s) % n) for i in range(n)]))
    return place(pieces, me, n, 0)


def butterfly_sum(v, axis, n):
    step = 1
    while step < n:
        v = v + lax.ppermute(v, axis, [(i, i ^ step) for i in range(n)])
        step *= 2
    return v


def build_local(nx, nz):
    nc = nx * nz

    def col_of_rho(rho):
        return (rho % nx) * nz + rho // nx

    perms, regions = [], np.zeros((nc, 3), np.int32)
    for j in range(3):
        pairs = []
        for src in range(nc):
            rho = (3 * src + j) % nc
            regions[rho, j] = (3 * src + j) // nc
            pairs.append((src, col_of_rho(rho)))
        perms.append(pairs)
    assert all(sorted(regions[r]) == [0, 1, 2] for r in range(nc))

    def head_table(width):
        piece = width // nc
        off = np.zeros((nc, 2), np.int32)
        owner = []
        for rho in range(nc):
            lo, hi = piece * rho, piece * (rho + 1)
            hs = [h for h in range(ATTENTION_HEADS) if lo <= h * HEAD_WIDTH < hi]
            assert 1 <= len(hs) <= 2
            for slot in range(2):
                o = (hs[0] + slot) * HEAD_WIDTH - lo
                off[rho, slot] = min(o, piece)
            for slot, h in enumerate(hs):
                owner.append((h, col_of_rho(rho), slot))
        owner.sort()
        assert [o[0] for o in owner] == list(range(ATTENTION_HEADS))
        gather = np.array([c * 2 + s for _, c, s in owner], np.int32)
        return off, gather

    shift_pairs = [(col_of_rho(r + 1), col_of_rho(r)) for r in range(nc - 1)]

    def body(tokens, w_qkv, q_gain, k_gain, segment_ids):
        tok_blk, feat_blk = tokens.shape
        width = q_gain.shape[0]
        piece = width // nc
        quarter = tok_blk // nx
        pack_tokens = segment_ids.shape[1]
        x = lax.axis_index("x")
        z = lax.axis_index("z")
        rho = z * nx + x
        off_tab, gather_idx = head_table(width)

        wp = w_qkv.reshape(feat_blk, 3, piece)
        got = [lax.ppermute(wp[:, j, :], COL, perms[j]) for j in range(3)]
        reg = jnp.asarray(regions)[rho]
        wr = []
        for s in range(3):
            acc = jnp.where(reg[0] == s, got[0], got[1])
            acc = jnp.where(reg[2] == s, got[2], acc)
            wr.append(acc)
        wr = jnp.stack(wr, axis=0)
        pieces = [wr] + [lax.ppermute(wr, "x", [(i, (i + s) % nx) for i in range(nx)]) for s in range(1, nx)]
        cols = []
        for reg_i in range(3):
            for j in range(nx):
                acc = pieces[0][reg_i]
                for s in range(1, nx):
                    acc = jnp.where((x - s) % nx == j, pieces[s][reg_i], acc)
                cols.append(acc)
        wg = jnp.concatenate(cols, axis=1)

        tq = tokens.reshape(nx, quarter, feat_blk)
        tq = shift_all_to_all(tq, "x", nx, x)
        n_packs = nc // 2
        half = quarter // 2
        qg = lax.dynamic_slice_in_dim(q_gain, z * nx * piece, nx * piece)
        kg = lax.dynamic_slice_in_dim(k_gain, z * nx * piece, nx * piece)
        done = []
        for tc in range(2):
          th = tq[:, tc * half:(tc + 1) * half]
          th = shift_gather(th, "z", nz, z, 1)
          th = th.reshape(n_packs, 2 * half, feat_blk)
          part = jnp.einsum("ptf,fc->ptc", th, wg, preferred_element_type=jnp.float32)
          part = part.astype(jnp.bfloat16)
          mine = lax.psum_scatter(part, ROW, scatter_dimension=0, tiled=True)[0]
          mine = mine.reshape(2 * half, 3, nx * piece)
          mine, qgc, kgc, xc = lax.optimization_barrier((mine, qg, kg, x))

          qv = mine[:, 0, :].astype(jnp.float32)
          kv = mine[:, 1, :].astype(jnp.float32)
          sums = jnp.stack([jnp.sum(qv * qv, axis=-1), jnp.sum(kv * kv, axis=-1)], axis=-1)
          sums = butterfly_sum(sums, "z", nz)
          rs = lax.rsqrt(sums / width + 1e-06)
          nq = (qv * rs[:, 0:1] * qgc).astype(jnp.bfloat16)
          nk = (kv * rs[:, 1:2] * kgc).astype(jnp.bfloat16)
          normed = jnp.stack([nq, nk, mine[:, 2, :]], axis=1)

          normed = normed.reshape(2 * half, 3, nx, piece)
          got = shift_all_to_all(jnp.moveaxis(normed, 2, 0), "x", nx, xc)
          ext = lax.ppermute(got[..., :HEAD_WIDTH], COL, shift_pairs)
          got = jnp.concatenate([got, ext], axis=-1)
          done.append(got.reshape(nx, 2, half, 3, piece + HEAD_WIDTH))
        sl = jnp.stack(done, axis=2).reshape(pack_tokens, 3, piece + HEAD_WIDTH)

        offs = jnp.asarray(off_tab)[rho]
        heads = jnp.stack(
            [lax.dynamic_slice_in_dim(sl, offs[i], HEAD_WIDTH, axis=2) for i in range(2)], axis=2
        )
        ids = segment_ids[0].reshape(2, nx, quarter).transpose(1, 0, 2).reshape(pack_tokens)
        mask = ids[:, None] == ids[None, :]
        tpc = pack_tokens // nc
        backs = []
        for slot in range(2):
            q3 = heads[:, 0, slot]
            k3 = heads[:, 1, slot]
            v3 = heads[:, 2, slot]
            scores = jnp.einsum("qd,kd->qk", q3, k3, preferred_element_type=jnp.float32)
            scores = scores * HEAD_WIDTH ** (-0.5)
            masked = jnp.where(mask, scores, -1e30)
            top = jnp.max(masked, axis=-1, keepdims=True)
            expo = jnp.where(mask, jnp.exp(masked - top), 0.0)
            total = jnp.sum(expo, axis=-1)
            weights = expo.astype(jnp.bfloat16)
            summed = jnp.einsum("qk,kd->qd", weights, v3, preferred_element_type=jnp.float32)
            res = (summed / total[:, None]).astype(jnp.bfloat16)
            res = res.reshape(nx, 2, quarter // tpc, tpc, HEAD_WIDTH)
            res = jnp.transpose(res, (1, 0, 2, 3, 4)).reshape(nc, tpc, HEAD_WIDTH)
            backs.append(lax.all_to_all(res, COL, 0, 0, tiled=True))
        back = jnp.stack(backs, axis=1).reshape(nc * 2, tpc, HEAD_WIDTH)
        out = jnp.take(back, jnp.asarray(gather_idx), axis=0)
        return jnp.transpose(out, (1, 0, 2)).reshape(tpc, width)

    return body


def solution(mesh):
    nr, nc = mesh.devices.shape
    nx = 4
    nz = nc // nx
    m4 = Mesh(mesh.devices.reshape(nr // 2, 2, nx, nz), ("y", "k", "x", "z"))
    return jax.shard_map(
        build_local(nx, nz),
        mesh=m4,
        in_specs=(P(COL, ROW), P(ROW, COL), P(), P(), P(ROW, None)),
        out_specs=P(ROW + COL, None),
        check_vma=False,
    )
```

```python
import numpy as np
import jax
import jax.numpy as jnp
from jax import lax
from jax.sharding import Mesh, PartitionSpec as P

ATTENTION_HEADS = 25
HEAD_WIDTH = 128
ROW = ("y", "k")
COL = ("x", "z")


def place(pieces, me, n, dim):
    outs = []
    for j in range(n):
        acc = pieces[0]
        for s in range(1, n):
            acc = jnp.where((me - s) % n == j, pieces[s], acc)
        outs.append(acc)
    return jnp.stack(outs, dim)


def shift_gather(v, axis, n, me, dim):
    pieces = [v] + [lax.ppermute(v, axis, [(i, (i + s) % n) for i in range(n)]) for s in range(1, n)]
    return place(pieces, me, n, dim)


def shift_all_to_all(v, axis, n, me):
    pieces = [lax.dynamic_index_in_dim(v, me, 0, False)]
    for s in range(1, n):
        piece = lax.dynamic_index_in_dim(v, (me + s) % n, 0, False)
        pieces.append(lax.ppermute(piece, axis, [(i, (i + s) % n) for i in range(n)]))
    return place(pieces, me, n, 0)


def butterfly_sum(v, axis, n):
    step = 1
    while step < n:
        v = v + lax.ppermute(v, axis, [(i, i ^ step) for i in range(n)])
        step *= 2
    return v


def build_local(nx, nz):
    nc = nx * nz

    def col_of_rho(rho):
        return (rho % nx) * nz + rho // nx

    perms, regions = [], np.zeros((nc, 3), np.int32)
    for j in range(3):
        pairs = []
        for src in range(nc):
            rho = (3 * src + j) % nc
            regions[rho, j] = (3 * src + j) // nc
            pairs.append((src, col_of_rho(rho)))
        perms.append(pairs)
    assert all(sorted(regions[r]) == [0, 1, 2] for r in range(nc))

    def head_table(width):
        piece = width // nc
        off = np.zeros((nc, 2), np.int32)
        owner = []
        for rho in range(nc):
            lo, hi = piece * rho, piece * (rho + 1)
            hs = [h for h in range(ATTENTION_HEADS) if lo <= h * HEAD_WIDTH < hi]
            assert 1 <= len(hs) <= 2
            for slot in range(2):
                o = (hs[0] + slot) * HEAD_WIDTH - lo
                off[rho, slot] = min(o, piece)
            for slot, h in enumerate(hs):
                owner.append((h, col_of_rho(rho), slot))
        owner.sort()
        assert [o[0] for o in owner] == list(range(ATTENTION_HEADS))
        gather = np.array([c * 2 + s for _, c, s in owner], np.int32)
        return off, gather

    shift_pairs = [(col_of_rho(r + 1), col_of_rho(r)) for r in range(nc - 1)]

    def body(tokens, w_qkv, q_gain, k_gain, segment_ids):
        tok_blk, feat_blk = tokens.shape
        width = q_gain.shape[0]
        piece = width // nc
        quarter = tok_blk // nx
        pack_tokens = segment_ids.shape[1]
        x = lax.axis_index("x")
        z = lax.axis_index("z")
        rho = z * nx + x
        off_tab, gather_idx = head_table(width)

        wp = w_qkv.reshape(feat_blk, 3, piece)
        got = [lax.ppermute(wp[:, j, :], COL, perms[j]) for j in range(3)]
        reg = jnp.asarray(regions)[rho]
        wr = []
        for s in range(3):
            acc = jnp.where(reg[0] == s, got[0], got[1])
            acc = jnp.where(reg[2] == s, got[2], acc)
            wr.append(acc)
        wr = jnp.stack(wr, axis=0)
        pieces = [wr] + [lax.ppermute(wr, "x", [(i, (i + s) % nx) for i in range(nx)]) for s in range(1, nx)]
        cols = []
        for reg_i in range(3):
            for j in range(nx):
                acc = pieces[0][reg_i]
                for s in range(1, nx):
                    acc = jnp.where((x - s) % nx == j, pieces[s][reg_i], acc)
                cols.append(acc)
        wg = jnp.concatenate(cols, axis=1)

        tq = tokens.reshape(nx, quarter, feat_blk)
        tq = shift_all_to_all(tq, "x", nx, x)
        n_packs = nc // 2
        half = quarter // 2
        qg = lax.dynamic_slice_in_dim(q_gain, z * nx * piece, nx * piece)
        kg = lax.dynamic_slice_in_dim(k_gain, z * nx * piece, nx * piece)
        done = []
        for tc in range(2):
          th = tq[:, tc * half:(tc + 1) * half]
          th = shift_gather(th, "z", nz, z, 1)
          th = th.reshape(n_packs, 2 * half, feat_blk)
          part = jnp.einsum("ptf,fc->ptc", th, wg, preferred_element_type=jnp.float32)
          part = part.astype(jnp.bfloat16)
          mine = lax.psum_scatter(part, ROW, scatter_dimension=0, tiled=True)[0]
          mine = mine.reshape(2 * half, 3, nx * piece)
          mine, qgc, kgc, xc = lax.optimization_barrier((mine, qg, kg, x))

          qv = mine[:, 0, :].astype(jnp.float32)
          kv = mine[:, 1, :].astype(jnp.float32)
          sums = jnp.stack([jnp.sum(qv * qv, axis=-1), jnp.sum(kv * kv, axis=-1)], axis=-1)
          sums = butterfly_sum(sums, "z", nz)
          rs = lax.rsqrt(sums / width + 1e-06)
          nq = (qv * rs[:, 0:1] * qgc).astype(jnp.bfloat16)
          nk = (kv * rs[:, 1:2] * kgc).astype(jnp.bfloat16)
          normed = jnp.stack([nq, nk, mine[:, 2, :]], axis=1)

          normed = normed.reshape(2 * half, 3, nx, piece)
          got = shift_all_to_all(jnp.moveaxis(normed, 2, 0), "x", nx, xc)
          ext = lax.ppermute(got[..., :HEAD_WIDTH], COL, shift_pairs)
          got = jnp.concatenate([got, ext], axis=-1)
          done.append(got.reshape(nx, 2, half, 3, piece + HEAD_WIDTH))
        sl = jnp.stack(done, axis=2).reshape(pack_tokens, 3, piece + HEAD_WIDTH)

        offs = jnp.asarray(off_tab)[rho]
        heads = jnp.stack(
            [lax.dynamic_slice_in_dim(sl, offs[i], HEAD_WIDTH, axis=2) for i in range(2)], axis=2
        )
        q3 = heads[:, 0]
        k3 = heads[:, 1]
        v3 = heads[:, 2]

        ids = segment_ids[0].reshape(2, nx, quarter).transpose(1, 0, 2).reshape(pack_tokens)
        mask = (ids[:, None] == ids[None, :])[None]
        scores = jnp.einsum("qhd,khd->hqk", q3, k3, preferred_element_type=jnp.float32)
        scores = scores * HEAD_WIDTH ** (-0.5)
        masked = jnp.where(mask, scores, -1e30)
        top = jnp.max(masked, axis=-1, keepdims=True)
        expo = jnp.where(mask, jnp.exp(masked - top), 0.0)
        total = jnp.sum(expo, axis=-1)
        weights = expo.astype(jnp.bfloat16)
        summed = jnp.einsum("hqk,khd->hqd", weights, v3, preferred_element_type=jnp.float32)
        res = (summed / total[..., None]).astype(jnp.bfloat16)

        tpc = pack_tokens // nc
        res = res.reshape(2, nx, 2, quarter // tpc, tpc, HEAD_WIDTH)
        res = jnp.transpose(res, (2, 1, 3, 4, 0, 5)).reshape(nc, tpc, 2, HEAD_WIDTH)
        back = lax.all_to_all(res, COL, 0, 0, tiled=True)
        back = jnp.transpose(back, (0, 2, 1, 3)).reshape(nc * 2, tpc, HEAD_WIDTH)
        out = jnp.take(back, jnp.asarray(gather_idx), axis=0)
        return jnp.transpose(out, (1, 0, 2)).reshape(tpc, width)

    return body


def solution(mesh):
    nr, nc = mesh.devices.shape
    nx = 4
    nz = nc // nx
    m4 = Mesh(mesh.devices.reshape(nr // 2, 2, nx, nz), ("y", "k", "x", "z"))
    return jax.shard_map(
        build_local(nx, nz),
        mesh=m4,
        in_specs=(P(COL, ROW), P(ROW, COL), P(), P(), P(ROW, None)),
        out_specs=P(ROW + COL, None),
        check_vma=False,
    )
```
